256 devices in a mesh: outer: 4 (over x_lo, core), inner: 64 (over y, z, x_hi).
Axes of the slice: x: 4 (x_hi: 2, x_lo: 2; x = x_hi * 2 + x_lo), y: 4, z: 8, core: 2. Of those that a mesh axis runs over, the one named last changes fastest.
Arguments:
- queue: bfloat16 [1048576, 512], P(('outer', 'inner')), may hold values from -100 to 100
- pred: bfloat16 [32768, 512], P(('outer', 'inner')), may hold values from -1 to 1
- owner: int32 [32768, 1], P(('outer', 'inner')), may hold values from 0 to 255, as said below
- slot: int32 [32768], P(('outer', 'inner')), may hold values from 0 to 4095
Outputs:
- grad_pred: float32 [32768, 512], P(('outer', 'inner'))
The draws below stay inside these ranges and needn't reach their ends.
Inputs may be any that keep to these rules, and one draw needn't show every extreme that they name: Queue shard o lies on the device of outer index o // 64 and inner index o % 64. Among the rows of one device (aligned blocks of 128 rows), at most 4 name owners of one inner index; among the rows of one outer group (aligned blocks of 8192 rows), at most 64 name the same owner.
All inputs are finite; a program needn't handle non-finite values.
Results may differ from the reference program's by a relative error of at most 0.012.
Values may be sent and summed in bfloat16 or wider, within the bound.
No kernel may reach another device: no remote copies, remote signals or barrier semaphores. Data moves between devices by JAX's collectives and lax.ppermute only.
A program may use at most 128 MiB of HBM per device.

```python
import math
import jax
import jax.numpy as jnp
from jax import lax

D = 512
ROW_DEV = 128
QROW_DEV = 4096
BATCH = 32768
QUEUE = 1048576
CAP_MEMBER = 4
N_OUTER = 4
N_INNER = 64
DEVICES = 256


def owner_table(key):
    k_hot, k_pick, k_order, k_tiebreak, k_offset = jax.random.split(jax.random.fold_in(key, 11), 5)
    slots_dev = N_INNER * CAP_MEMBER
    hot_count = max(1, ROW_DEV // (4 * CAP_MEMBER))
    hot_member = (jax.random.permutation(k_hot, N_INNER).astype(jnp.int32) < hot_count).astype(jnp.int32)
    hot_slot = jnp.repeat(hot_member, CAP_MEMBER)[None, :]
    jitter = jax.vmap(lambda subkey: jax.random.permutation(subkey, slots_dev))(jax.random.split(k_pick, DEVICES)).astype(jnp.int32)
    priority = hot_slot * slots_dev + jitter
    unused, chosen = lax.top_k(priority, ROW_DEV)
    member = (chosen // CAP_MEMBER).astype(jnp.int32)
    shuffle = jax.vmap(lambda subkey: jax.random.permutation(subkey, ROW_DEV))(jax.random.split(k_order, DEVICES)).astype(jnp.int32)
    member = jnp.take_along_axis(member, shuffle, 1)
    group_rows = N_INNER * ROW_DEV
    member = member.reshape(N_OUTER, group_rows)
    tiebreak = jax.vmap(lambda subkey: jax.random.permutation(subkey, group_rows))(jax.random.split(k_tiebreak, N_OUTER)).astype(jnp.int32)
    sort_order = jnp.argsort(member * group_rows + tiebreak, axis=1).astype(jnp.int32)
    sorted_member = jnp.take_along_axis(member, sort_order, 1)
    counts = jnp.sum((member[:, :, None] == jnp.arange(N_INNER, dtype=jnp.int32)[None, None, :]).astype(jnp.int32), 1)
    starts = jnp.cumsum(counts, 1) - counts
    class_rank = jnp.arange(group_rows, dtype=jnp.int32)[None, :] - jnp.take_along_axis(starts, sorted_member, 1)
    shift_by = jax.random.randint(k_offset, (N_OUTER, N_INNER), 0, N_OUTER, dtype=jnp.int32)
    sorted_group = (class_rank + jnp.take_along_axis(shift_by, sorted_member, 1)) % N_OUTER
    inverse_order = jnp.argsort(sort_order, axis=1).astype(jnp.int32)
    group_part = jnp.take_along_axis(sorted_group, inverse_order, 1)
    return (group_part * N_INNER + member).reshape(BATCH).astype(jnp.int32)


def slot_table(key):
    return jax.random.randint(jax.random.fold_in(key, 23), (BATCH,), 0, QROW_DEV, dtype=jnp.int32)


def queue_rows(key, rows):
    k_center, k_cluster, k_jitter = jax.random.split(jax.random.fold_in(key, 31), 3)
    cluster_count = max(4, BATCH // 8)
    mixing = 3.0
    centers = jax.random.normal(k_center, (cluster_count, D), jnp.float32)
    cluster_id = jax.vmap(lambda row_index: jax.random.randint(jax.random.fold_in(k_cluster, row_index), (), 0, cluster_count, dtype=jnp.int32))(rows)
    jitter = jax.vmap(lambda row_index: jax.random.normal(jax.random.fold_in(k_jitter, row_index), (D,), jnp.float32))(rows)
    values = mixing * centers[cluster_id] + jitter
    energy = mixing * mixing + 1.0
    return (jnp.clip(values, -100.0, 100.0), energy)


def draw_queue(key, part):
    values, energy = queue_rows(key, jnp.arange(QUEUE, dtype=jnp.int32))
    return values.astype(jnp.bfloat16)


def draw_owner(key, part):
    return owner_table(key).reshape(BATCH, 1)


def draw_slot(key, part):
    return slot_table(key)


def draw_pred(key, part):
    rows = owner_table(key) * QROW_DEV + slot_table(key)
    source_rows, energy = queue_rows(key, rows)
    k_align, k_jitter = jax.random.split(jax.random.fold_in(key, 47))
    alignment = jax.random.uniform(k_align, (BATCH, 1), jnp.float32, 0.5, 3.0)
    jitter = jax.random.normal(k_jitter, (BATCH, D), jnp.float32)
    factor = 0.05 * lax.rsqrt(alignment * alignment * energy + 1.0)
    return jnp.clip((alignment * source_rows + jitter) * factor, -1.0, 1.0).astype(jnp.bfloat16)


def setup_inputs(seed: int = 0) -> dict:
    arg_keys = jax.random.split(jax.random.key(seed), 5)
    queue = draw_queue(jax.random.fold_in(arg_keys[4], 71), 0)
    pred = draw_pred(jax.random.fold_in(arg_keys[4], 71), 0)
    owner = draw_owner(jax.random.fold_in(arg_keys[4], 71), 0)
    slot = draw_slot(jax.random.fold_in(arg_keys[4], 71), 0)
    return {"queue": queue, "pred": pred, "owner": owner, "slot": slot}


EPS = 1e-06
INV_TAU = 10.0

def reference(queue, pred, owner, slot):
    index_rows = owner[:, 0] * QROW_DEV + slot
    fetched = queue[index_rows].astype(jnp.float32)
    neighbour = (fetched * lax.rsqrt(lax.optimization_barrier(jnp.sum(fetched * fetched, 1, keepdims=True)) + EPS)).astype(jnp.bfloat16)
    predicted = pred.astype(jnp.float32)
    inverse = lax.rsqrt(lax.optimization_barrier(jnp.sum(predicted * predicted, 1, keepdims=True)) + EPS)
    queries = (predicted * inverse).astype(jnp.bfloat16)
    block_rows = math.gcd(BATCH, 1024)
    block_count = BATCH // block_rows
    row_pieces = neighbour.reshape(block_count, block_rows, D)
    column_ids = jnp.arange(BATCH, dtype=jnp.int32)

    def first_pass(column_total, row_piece):
        exponent = jnp.exp(jnp.einsum('rd,cd->rc', row_piece, queries, preferred_element_type=jnp.float32) * INV_TAU)
        return (column_total + lax.optimization_barrier(jnp.sum(exponent, 0)), lax.optimization_barrier(jnp.sum(exponent, 1)))
    column_total, row_total = lax.scan(first_pass, jnp.zeros((BATCH,), jnp.float32), row_pieces)

    def second_pass(dquery, entry_item):
        row_piece, row_part, block_index = entry_item
        exponent = jnp.exp(jnp.einsum('rd,cd->rc', row_piece, queries, preferred_element_type=jnp.float32) * INV_TAU)
        row_ids = block_index * block_rows + jnp.arange(block_rows, dtype=jnp.int32)
        diagonal = (row_ids[:, None] == column_ids[None, :]).astype(jnp.float32)
        weights = (0.5 * (exponent / row_part[:, None] + exponent / column_total[None, :]) - diagonal).astype(jnp.bfloat16)
        product = lax.dot_general(weights, row_piece, (((0,), (0,)), ((), ())), preferred_element_type=jnp.float32)
        return (dquery + product, 0)
    dquery, unused = lax.scan(second_pass, jnp.zeros((BATCH, D), jnp.float32), (row_pieces, row_total, jnp.arange(block_count, dtype=jnp.int32)))
    dquery = dquery * INV_TAU
    radial = lax.optimization_barrier(jnp.sum(predicted * dquery, 1, keepdims=True))
    return inverse * dquery - predicted * inverse * inverse * inverse * radial
```

```python
import jax
import jax.numpy as jnp
import numpy as np
from jax import lax
from jax.sharding import Mesh
from jax.sharding import PartitionSpec as P

EPS = 1e-06
INV_TAU = 10.0

ALL = ("xl", "c", "y", "z", "xh")
INNER = ("y", "z", "xh")
OUTER = ("xl", "c")
ROWS = ("c", "y", "z")
COLS = ("xl", "xh")


def block_exp(row_block, column_block):
    return jnp.exp(
        jnp.einsum("rd,cd->rc", row_block, column_block, preferred_element_type=jnp.float32)
        * INV_TAU
    )


def mixed_weights(exponent, row_total, column_total, row_first, column_first, rows_dev):
    row_offset = jnp.arange(exponent.shape[0], dtype=jnp.int32)[:, None] - row_first
    column_offset = jnp.arange(exponent.shape[1], dtype=jnp.int32)[None, :] - column_first
    diagonal = ((row_offset == column_offset) & (row_offset >= 0) & (row_offset < rows_dev)).astype(
        jnp.float32
    )
    return (
        0.5 * (exponent / row_total[:, None] + exponent / column_total[None, :]) - diagonal
    ).astype(jnp.bfloat16)


def column_terms(weights, row_block):
    return lax.dot_general(
        weights, row_block, (((0,), (0,)), ((), ())), preferred_element_type=jnp.float32
    )


def tree_sum(value, axes):
    for axis in axes:
        size = lax.axis_size(axis)
        step = 1
        while step < size:
            pairs = [(i, i ^ step) for i in range(size)]
            value = value + lax.ppermute(value, axis, pairs)
            step *= 2
    return value


def fetch_rows(queue, owner, slot):
    outer_count = lax.axis_size(OUTER)
    inner_count = lax.axis_size(INNER)
    rows_dev = slot.shape[0]
    feature_width = queue.shape[1]
    cap_member = max(2, 2 * rows_dev // inner_count)
    cap_group = inner_count * cap_member // outer_count
    owners_of = owner[:, 0]
    owner_member = owners_of % inner_count
    owner_group = owners_of // inner_count
    position = jnp.arange(rows_dev, dtype=jnp.int32)
    earlier = (owner_member[:, None] == owner_member[None, :]) & (
        position[None, :] < position[:, None]
    )
    member_place = owner_member * cap_member + jnp.sum(earlier.astype(jnp.int32), 1)
    request = jnp.stack(
        [
            jnp.full((inner_count * cap_member,), -1, jnp.int32).at[member_place].set(slot),
            jnp.full((inner_count * cap_member,), outer_count, jnp.int32)
            .at[member_place]
            .set(owner_group),
        ],
        1,
    ).reshape(inner_count, cap_member, 2)
    relay = lax.all_to_all(request, INNER, split_axis=0, concat_axis=0, tiled=True)
    relay_slot = relay[:, :, 0].reshape(-1)
    relay_group = relay[:, :, 1].reshape(-1)
    entry_index = jnp.arange(relay_slot.shape[0], dtype=jnp.int32)
    ahead = (relay_group[:, None] == relay_group[None, :]) & (
        entry_index[None, :] < entry_index[:, None]
    )
    group_place = relay_group * cap_group + jnp.sum(ahead.astype(jnp.int32), 1)
    asking = (
        jnp.full((outer_count * cap_group,), -1, jnp.int32)
        .at[group_place]
        .set(relay_slot, mode="drop")
    )
    asking = asking.reshape(outer_count, cap_group)
    asked = lax.all_to_all(asking, OUTER, split_axis=0, concat_axis=0, tiled=True)
    looked = jnp.take(queue, jnp.maximum(asked, 0), axis=0)
    looked = jnp.where((asked >= 0)[..., None], looked, jnp.zeros((), jnp.bfloat16))
    answered = lax.all_to_all(looked, OUTER, split_axis=0, concat_axis=0, tiled=True)
    answered = answered.reshape(outer_count * cap_group, feature_width)
    relayed = jnp.take(answered, jnp.minimum(group_place, outer_count * cap_group - 1), axis=0)
    relayed = jnp.where((relay_slot >= 0)[:, None], relayed, jnp.zeros((), jnp.bfloat16))
    relayed = relayed.reshape(inner_count, cap_member, feature_width)
    returned = lax.all_to_all(relayed, INNER, split_axis=0, concat_axis=0, tiled=True)
    return jnp.take(
        returned.reshape(inner_count * cap_member, feature_width), member_place, axis=0
    ).astype(jnp.float32)


def shards(queue, pred, owner, slot):
    rows_dev = pred.shape[0]
    fetched = fetch_rows(queue, owner, slot)
    neighbour = (fetched * lax.rsqrt(jnp.sum(fetched * fetched, 1, keepdims=True) + EPS)).astype(
        jnp.bfloat16
    )
    predicted = pred.astype(jnp.float32)
    inverse = lax.rsqrt(jnp.sum(predicted * predicted, 1, keepdims=True) + EPS)
    queries = (predicted * inverse).astype(jnp.bfloat16)
    row_at = lax.axis_index(ROWS)
    column_at = lax.axis_index(COLS)
    row_block = lax.all_gather(neighbour, ROWS, axis=0, tiled=True)
    exponent = block_exp(row_block, lax.all_gather(queries, COLS, axis=0, tiled=True))
    row_total = tree_sum(jnp.sum(exponent, 1), ROWS)
    column_total = lax.psum(jnp.sum(exponent, 0), COLS)
    weights = mixed_weights(
        exponent, row_total, column_total, row_at * rows_dev, column_at * rows_dev, rows_dev
    )
    dquery = lax.psum_scatter(
        column_terms(weights, row_block), COLS, scatter_dimension=0, tiled=True
    )
    dquery = dquery * INV_TAU
    radial = jnp.sum(predicted * dquery, 1, keepdims=True)
    return inverse * dquery - predicted * inverse * inverse * inverse * radial


def solution(mesh):
    axes = dict(zip(mesh.axis_names, mesh.devices.shape))
    outer, inner = axes["outer"], axes["inner"]
    fine = Mesh(
        np.asarray(mesh.devices).reshape(2, outer // 2, inner // 16, 8, 2), ALL
    )
    spec = P(ALL, None)
    in_specs = (spec, spec, spec, P(ALL))
    return jax.shard_map(shards, mesh=fine, in_specs=in_specs, out_specs=spec, check_vma=False)
```

```python
import jax
import jax.numpy as jnp
import numpy as np
from jax import lax
from jax.sharding import Mesh
from jax.sharding import PartitionSpec as P

EPS = 1e-06
INV_TAU = 10.0

ALL = ("xl", "c", "y", "z", "xh")
INNER = ("y", "z", "xh")
OUTER = ("xl", "c")
ROWS = ("c", "y", "z")
COLS = ("xl", "xh")


def block_exp(row_block, column_block):
    return jnp.exp(
        jnp.einsum("rd,cd->rc", row_block, column_block, preferred_element_type=jnp.float32)
        * INV_TAU
    )


def mixed_weights(exponent, row_total, column_total, row_first, column_first, rows_dev):
    row_offset = jnp.arange(exponent.shape[0], dtype=jnp.int32)[:, None] - row_first
    column_offset = jnp.arange(exponent.shape[1], dtype=jnp.int32)[None, :] - column_first
    diagonal = ((row_offset == column_offset) & (row_offset >= 0) & (row_offset < rows_dev)).astype(
        jnp.float32
    )
    return (
        0.5 * (exponent / row_total[:, None] + exponent / column_total[None, :]) - diagonal
    ).astype(jnp.bfloat16)


def column_terms(weights, row_block):
    return lax.dot_general(
        weights, row_block, (((0,), (0,)), ((), ())), preferred_element_type=jnp.float32
    )


def tree_sum(value, axes):
    for axis in axes:
        size = lax.axis_size(axis)
        step = 1
        while step < size:
            pairs = [(i, i ^ step) for i in range(size)]
            value = value + lax.ppermute(value, axis, pairs)
            step *= 2
    return value


def fetch_rows(queue, owner, slot):
    outer_count = lax.axis_size(OUTER)
    inner_count = lax.axis_size(INNER)
    rows_dev = slot.shape[0]
    feature_width = queue.shape[1]
    cap_member = max(2, 2 * rows_dev // inner_count)
    cap_group = inner_count * cap_member // outer_count
    owners_of = owner[:, 0]
    owner_member = owners_of % inner_count
    owner_group = owners_of // inner_count
    position = jnp.arange(rows_dev, dtype=jnp.int32)
    earlier = (owner_member[:, None] == owner_member[None, :]) & (
        position[None, :] < position[:, None]
    )
    member_place = owner_member * cap_member + jnp.sum(earlier.astype(jnp.int32), 1)
    request = jnp.stack(
        [
            jnp.full((inner_count * cap_member,), -1, jnp.int32).at[member_place].set(slot),
            jnp.full((inner_count * cap_member,), outer_count, jnp.int32)
            .at[member_place]
            .set(owner_group),
        ],
        1,
    ).reshape(inner_count, cap_member, 2)
    relay = lax.all_to_all(request, INNER, split_axis=0, concat_axis=0, tiled=True)
    relay_slot = relay[:, :, 0].reshape(-1)
    relay_group = relay[:, :, 1].reshape(-1)
    entry_index = jnp.arange(relay_slot.shape[0], dtype=jnp.int32)
    ahead = (relay_group[:, None] == relay_group[None, :]) & (
        entry_index[None, :] < entry_index[:, None]
    )
    group_place = relay_group * cap_group + jnp.sum(ahead.astype(jnp.int32), 1)
    asking = (
        jnp.full((outer_count * cap_group,), -1, jnp.int32)
        .at[group_place]
        .set(relay_slot, mode="drop")
    )
    asking = asking.reshape(outer_count, cap_group)
    asked = lax.all_to_all(asking, OUTER, split_axis=0, concat_axis=0, tiled=True)
    looked = jnp.take(queue, jnp.maximum(asked, 0), axis=0)
    looked = jnp.where((asked >= 0)[..., None], looked, jnp.zeros((), jnp.bfloat16))
    answered = lax.all_to_all(looked, OUTER, split_axis=0, concat_axis=0, tiled=True)
    answered = answered.reshape(outer_count * cap_group, feature_width)
    relayed = jnp.take(answered, jnp.minimum(group_place, outer_count * cap_group - 1), axis=0)
    relayed = jnp.where((relay_slot >= 0)[:, None], relayed, jnp.zeros((), jnp.bfloat16))
    relayed = relayed.reshape(inner_count, cap_member, feature_width)
    returned = lax.all_to_all(relayed, INNER, split_axis=0, concat_axis=0, tiled=True)
    return jnp.take(
        returned.reshape(inner_count * cap_member, feature_width), member_place, axis=0
    ).astype(jnp.float32)


def ring_pairs(size, step):
    return [(i, (i + step) % size) for i in range(size)]


def gather_columns(value, axes):
    size = lax.axis_size(axes)
    me = lax.axis_index(axes)
    parts = [value] + [lax.ppermute(value, axes, ring_pairs(size, k)) for k in range(1, size)]
    source = (me - jnp.arange(size, dtype=jnp.int32)) % size
    return jnp.take(jnp.stack(parts), source, axis=0).reshape((-1,) + value.shape[1:])


def scatter_columns(weights, row_block, axes, rows_dev):
    size = lax.axis_size(axes)
    me = lax.axis_index(axes)
    total = None
    for k in list(range(1, size)) + [0]:
        target = (me + k) % size
        piece = lax.dynamic_slice_in_dim(weights, target * rows_dev, rows_dev, axis=1)
        part = column_terms(piece, row_block)
        if k:
            part = lax.ppermute(part, axes, ring_pairs(size, k))
        total = part if total is None else total + part
    return total


def shards(queue, pred, owner, slot):
    rows_dev = pred.shape[0]
    fetched = fetch_rows(queue, owner, slot)
    neighbour = (fetched * lax.rsqrt(jnp.sum(fetched * fetched, 1, keepdims=True) + EPS)).astype(
        jnp.bfloat16
    )
    predicted = pred.astype(jnp.float32)
    inverse = lax.rsqrt(jnp.sum(predicted * predicted, 1, keepdims=True) + EPS)
    queries = (predicted * inverse).astype(jnp.bfloat16)
    row_at = lax.axis_index(ROWS)
    column_at = lax.axis_index(COLS)
    row_block = lax.all_gather(neighbour, ROWS, axis=0, tiled=True)
    exponent = block_exp(row_block, gather_columns(queries, COLS))
    row_total = tree_sum(jnp.sum(exponent, 1), ROWS)
    column_total = tree_sum(jnp.sum(exponent, 0), COLS)
    weights = mixed_weights(
        exponent, row_total, column_total, row_at * rows_dev, column_at * rows_dev, rows_dev
    )
    dquery = scatter_columns(weights, row_block, COLS, rows_dev)
    dquery = dquery * INV_TAU
    radial = jnp.sum(predicted * dquery, 1, keepdims=True)
    return inverse * dquery - predicted * inverse * inverse * inverse * radial


def solution(mesh):
    axes = dict(zip(mesh.axis_names, mesh.devices.shape))
    outer, inner = axes["outer"], axes["inner"]
    fine = Mesh(
        np.asarray(mesh.devices).reshape(2, outer // 2, inner // 16, 8, 2), ALL
    )
    spec = P(ALL, None)
    in_specs = (spec, spec, spec, P(ALL))
    return jax.shard_map(shards, mesh=fine, in_specs=in_specs, out_specs=spec, check_vma=False)
```

```python
import jax
import jax.numpy as jnp
import numpy as np
from jax import lax
from jax.sharding import Mesh
from jax.sharding import PartitionSpec as P

EPS = 1e-06
INV_TAU = 10.0

ALL = ("xl", "c", "y", "z", "xh")
INNER = ("y", "z", "xh")
OUTER = ("xl", "c")
ROWS = ("c", "y", "z")
COLS = ("xl", "xh")


def block_exp(row_block, column_block):
    return jnp.exp(
        jnp.einsum("rd,cd->rc", row_block, column_block, preferred_element_type=jnp.float32)
        * INV_TAU
    )


def mixed_weights(exponent, row_total, column_total, row_first, column_first, rows_dev):
    row_offset = jnp.arange(exponent.shape[0], dtype=jnp.int32)[:, None] - row_first
    column_offset = jnp.arange(exponent.shape[1], dtype=jnp.int32)[None, :] - column_first
    diagonal = ((row_offset == column_offset) & (row_offset >= 0) & (row_offset < rows_dev)).astype(
        jnp.float32
    )
    return (
        0.5 * (exponent / row_total[:, None] + exponent / column_total[None, :]) - diagonal
    ).astype(jnp.bfloat16)


def column_terms(weights, row_block):
    return lax.dot_general(
        weights, row_block, (((0,), (0,)), ((), ())), preferred_element_type=jnp.float32
    )


def tree_sum(value, axes):
    for axis in axes:
        size = lax.axis_size(axis)
        me = lax.axis_index(axis)
        parts = [value] + [lax.ppermute(value, axis, ring_pairs(size, k)) for k in range(1, size)]
        ordered = jnp.take(jnp.stack(parts), (me - jnp.arange(size, dtype=jnp.int32)) % size, axis=0)
        value = ordered[0]
        for k in range(1, size):
            value = value + ordered[k]
    return value


def fetch_rows(queue, owner, slot):
    outer_count = lax.axis_size(OUTER)
    inner_count = lax.axis_size(INNER)
    rows_dev = slot.shape[0]
    feature_width = queue.shape[1]
    cap_member = max(2, 2 * rows_dev // inner_count)
    cap_group = inner_count * cap_member // outer_count
    owners_of = owner[:, 0]
    owner_member = owners_of % inner_count
    owner_group = owners_of // inner_count
    position = jnp.arange(rows_dev, dtype=jnp.int32)
    earlier = (owner_member[:, None] == owner_member[None, :]) & (
        position[None, :] < position[:, None]
    )
    member_place = owner_member * cap_member + jnp.sum(earlier.astype(jnp.int32), 1)
    request = jnp.stack(
        [
            jnp.full((inner_count * cap_member,), -1, jnp.int32).at[member_place].set(slot),
            jnp.full((inner_count * cap_member,), outer_count, jnp.int32)
            .at[member_place]
            .set(owner_group),
        ],
        1,
    ).reshape(inner_count, cap_member, 2)
    relay = lax.all_to_all(request, INNER, split_axis=0, concat_axis=0, tiled=True)
    relay_slot = relay[:, :, 0].reshape(-1)
    relay_group = relay[:, :, 1].reshape(-1)
    entry_index = jnp.arange(relay_slot.shape[0], dtype=jnp.int32)
    ahead = (relay_group[:, None] == relay_group[None, :]) & (
        entry_index[None, :] < entry_index[:, None]
    )
    group_place = relay_group * cap_group + jnp.sum(ahead.astype(jnp.int32), 1)
    asking = (
        jnp.full((outer_count * cap_group,), -1, jnp.int32)
        .at[group_place]
        .set(relay_slot, mode="drop")
    )
    asking = asking.reshape(outer_count, cap_group)
    asked = lax.all_to_all(asking, OUTER, split_axis=0, concat_axis=0, tiled=True)
    looked = jnp.take(queue, jnp.maximum(asked, 0), axis=0)
    looked = jnp.where((asked >= 0)[..., None], looked, jnp.zeros((), jnp.bfloat16))
    answered = lax.all_to_all(looked, OUTER, split_axis=0, concat_axis=0, tiled=True)
    answered = answered.reshape(outer_count * cap_group, feature_width)
    relayed = jnp.take(answered, jnp.minimum(group_place, outer_count * cap_group - 1), axis=0)
    relayed = jnp.where((relay_slot >= 0)[:, None], relayed, jnp.zeros((), jnp.bfloat16))
    relayed = relayed.reshape(inner_count, cap_member, feature_width)
    returned = lax.all_to_all(relayed, INNER, split_axis=0, concat_axis=0, tiled=True)
    return jnp.take(
        returned.reshape(inner_count * cap_member, feature_width), member_place, axis=0
    ).astype(jnp.float32)


def ring_pairs(size, step):
    return [(i, (i + step) % size) for i in range(size)]


def gather_columns(value, axes):
    size = lax.axis_size(axes)
    me = lax.axis_index(axes)
    parts = [value] + [lax.ppermute(value, axes, ring_pairs(size, k)) for k in range(1, size)]
    source = (me - jnp.arange(size, dtype=jnp.int32)) % size
    return jnp.take(jnp.stack(parts), source, axis=0).reshape((-1,) + value.shape[1:])


def scatter_columns(weights, row_block, axes, rows_dev):
    size = lax.axis_size(axes)
    me = lax.axis_index(axes)
    terms = column_terms(weights, row_block)
    total = lax.dynamic_slice_in_dim(terms, me * rows_dev, rows_dev, axis=0)
    for k in range(1, size):
        target = (me + k) % size
        piece = lax.dynamic_slice_in_dim(terms, target * rows_dev, rows_dev, axis=0)
        total = total + lax.ppermute(piece, axes, ring_pairs(size, k))
    return total


def shards(queue, pred, owner, slot):
    rows_dev = pred.shape[0]
    fetched = fetch_rows(queue, owner, slot)
    neighbour = (fetched * lax.rsqrt(jnp.sum(fetched * fetched, 1, keepdims=True) + EPS)).astype(
        jnp.bfloat16
    )
    predicted = pred.astype(jnp.float32)
    inverse = lax.rsqrt(jnp.sum(predicted * predicted, 1, keepdims=True) + EPS)
    queries = (predicted * inverse).astype(jnp.bfloat16)
    row_at = lax.axis_index(ROWS)
    column_at = lax.axis_index(COLS)
    row_block = lax.all_gather(neighbour, ROWS, axis=0, tiled=True)
    exponent = block_exp(row_block, gather_columns(queries, COLS))
    row_total = tree_sum(jnp.sum(exponent, 1), ROWS)
    column_total = tree_sum(jnp.sum(exponent, 0), COLS)
    weights = mixed_weights(
        exponent, row_total, column_total, row_at * rows_dev, column_at * rows_dev, rows_dev
    )
    dquery = scatter_columns(weights, row_block, COLS, rows_dev)
    dquery = dquery * INV_TAU
    radial = jnp.sum(predicted * dquery, 1, keepdims=True)
    return inverse * dquery - predicted * inverse * inverse * inverse * radial


def solution(mesh):
    axes = dict(zip(mesh.axis_names, mesh.devices.shape))
    outer, inner = axes["outer"], axes["inner"]
    fine = Mesh(
        np.asarray(mesh.devices).reshape(2, outer // 2, inner // 16, 8, 2), ALL
    )
    spec = P(ALL, None)
    in_specs = (spec, spec, spec, P(ALL))
    return jax.shard_map(shards, mesh=fine, in_specs=in_specs, out_specs=spec, check_vma=False)
```

```python
import jax
import jax.numpy as jnp
import numpy as np
from jax import lax
from jax.sharding import Mesh
from jax.sharding import PartitionSpec as P

EPS = 1e-06
INV_TAU = 10.0

ALL = ("xl", "c", "y", "z", "xh")
INNER = ("y", "z", "xh")
OUTER = ("xl", "c")
ROWS = ("c", "y", "z")
COLS = ("xl", "xh")


def block_exp(row_block, column_block):
    return jnp.exp(
        jnp.einsum("rd,cd->rc", row_block, column_block, preferred_element_type=jnp.float32)
        * INV_TAU
    )


def mixed_weights(exponent, row_total, column_total, row_first, column_first, rows_dev):
    row_offset = jnp.arange(exponent.shape[0], dtype=jnp.int32)[:, None] - row_first
    column_offset = jnp.arange(exponent.shape[1], dtype=jnp.int32)[None, :] - column_first
    diagonal = ((row_offset == column_offset) & (row_offset >= 0) & (row_offset < rows_dev)).astype(
        jnp.float32
    )
    return (
        0.5 * (exponent / row_total[:, None] + exponent / column_total[None, :]) - diagonal
    ).astype(jnp.bfloat16)


def column_terms(weights, row_block):
    return lax.dot_general(
        weights, row_block, (((0,), (0,)), ((), ())), preferred_element_type=jnp.float32
    )


def tree_sum(value, axes):
    for axis in axes:
        size = lax.axis_size(axis)
        me = lax.axis_index(axis)
        parts = [value] + [lax.ppermute(value, axis, ring_pairs(size, k)) for k in range(1, size)]
        ordered = jnp.take(jnp.stack(parts), (me - jnp.arange(size, dtype=jnp.int32)) % size, axis=0)
        value = ordered[0]
        for k in range(1, size):
            value = value + ordered[k]
    return value


def fetch_rows(queue, owner, slot):
    outer_count = lax.axis_size(OUTER)
    inner_count = lax.axis_size(INNER)
    rows_dev = slot.shape[0]
    feature_width = queue.shape[1]
    cap_member = max(2, 2 * rows_dev // inner_count)
    cap_group = inner_count * cap_member // outer_count
    owners_of = owner[:, 0]
    owner_member = owners_of % inner_count
    owner_group = owners_of // inner_count
    position = jnp.arange(rows_dev, dtype=jnp.int32)
    earlier = (owner_member[:, None] == owner_member[None, :]) & (
        position[None, :] < position[:, None]
    )
    member_place = owner_member * cap_member + jnp.sum(earlier.astype(jnp.int32), 1)
    request = jnp.stack(
        [
            jnp.full((inner_count * cap_member,), -1, jnp.int32).at[member_place].set(slot),
            jnp.full((inner_count * cap_member,), outer_count, jnp.int32)
            .at[member_place]
            .set(owner_group),
        ],
        1,
    ).reshape(inner_count, cap_member, 2)
    relay = lax.all_to_all(request, INNER, split_axis=0, concat_axis=0, tiled=True)
    relay_slot = relay[:, :, 0].reshape(-1)
    relay_group = relay[:, :, 1].reshape(-1)
    entry_index = jnp.arange(relay_slot.shape[0], dtype=jnp.int32)
    ahead = (relay_group[:, None] == relay_group[None, :]) & (
        entry_index[None, :] < entry_index[:, None]
    )
    group_place = relay_group * cap_group + jnp.sum(ahead.astype(jnp.int32), 1)
    asking = (
        jnp.full((outer_count * cap_group,), -1, jnp.int32)
        .at[group_place]
        .set(relay_slot, mode="drop")
    )
    asking = asking.reshape(outer_count, cap_group)
    asked = lax.all_to_all(asking, OUTER, split_axis=0, concat_axis=0, tiled=True)
    looked = jnp.take(queue, jnp.maximum(asked, 0), axis=0)
    looked = jnp.where((asked >= 0)[..., None], looked, jnp.zeros((), jnp.bfloat16))
    answered = lax.all_to_all(looked, OUTER, split_axis=0, concat_axis=0, tiled=True)
    answered = answered.reshape(outer_count * cap_group, feature_width)
    relayed = jnp.take(answered, jnp.minimum(group_place, outer_count * cap_group - 1), axis=0)
    relayed = jnp.where((relay_slot >= 0)[:, None], relayed, jnp.zeros((), jnp.bfloat16))
    relayed = relayed.reshape(inner_count, cap_member, feature_width)
    returned = lax.all_to_all(relayed, INNER, split_axis=0, concat_axis=0, tiled=True)
    return jnp.take(
        returned.reshape(inner_count * cap_member, feature_width), member_place, axis=0
    ).astype(jnp.float32)


def ring_pairs(size, step):
    return [(i, (i + step) % size) for i in range(size)]


def gather_columns(value, axes):
    size = lax.axis_size(axes)
    parts = [value] + [lax.ppermute(value, axes, ring_pairs(size, k)) for k in range(1, size)]
    return jnp.concatenate(parts, axis=0)


def to_absolute(value, axes):
    size = lax.axis_size(axes)
    me = lax.axis_index(axes)
    pieces = value.reshape(size, -1)
    return jnp.take(pieces, (me - jnp.arange(size, dtype=jnp.int32)) % size, axis=0).reshape(-1)


def scatter_columns(exponent, row_total, column_total, row_block, row_first, axes, rows_dev):
    size = lax.axis_size(axes)
    total = None
    for k in list(range(1, size)) + [0]:
        columns = slice(k * rows_dev, (k + 1) * rows_dev)
        weights = mixed_weights(
            exponent[:, columns], row_total, column_total[columns], row_first, 0 if k == 0 else rows_dev, rows_dev
        )
        part = column_terms(weights, row_block)
        if k:
            part = lax.ppermute(part, axes, ring_pairs(size, size - k))
        total = part if total is None else total + part
    return total


def shards(queue, pred, owner, slot):
    rows_dev = pred.shape[0]
    fetched = fetch_rows(queue, owner, slot)
    neighbour = (fetched * lax.rsqrt(jnp.sum(fetched * fetched, 1, keepdims=True) + EPS)).astype(
        jnp.bfloat16
    )
    predicted = pred.astype(jnp.float32)
    inverse = lax.rsqrt(jnp.sum(predicted * predicted, 1, keepdims=True) + EPS)
    queries = (predicted * inverse).astype(jnp.bfloat16)
    row_at = lax.axis_index(ROWS)
    row_block = lax.all_gather(neighbour, ROWS, axis=0, tiled=True)
    exponent = block_exp(row_block, gather_columns(queries, COLS))
    row_total = tree_sum(jnp.sum(exponent, 1), ROWS)
    column_total = to_absolute(tree_sum(to_absolute(jnp.sum(exponent, 0), COLS), COLS), COLS)
    dquery = scatter_columns(
        exponent, row_total, column_total, row_block, row_at * rows_dev, COLS, rows_dev
    )
    dquery = dquery * INV_TAU
    radial = jnp.sum(predicted * dquery, 1, keepdims=True)
    return inverse * dquery - predicted * inverse * inverse * inverse * radial


def solution(mesh):
    axes = dict(zip(mesh.axis_names, mesh.devices.shape))
    outer, inner = axes["outer"], axes["inner"]
    fine = Mesh(
        np.asarray(mesh.devices).reshape(2, outer // 2, inner // 16, 8, 2), ALL
    )
    spec = P(ALL, None)
    in_specs = (spec, spec, spec, P(ALL))
    return jax.shard_map(shards, mesh=fine, in_specs=in_specs, out_specs=spec, check_vma=False)
```

```python
import jax
import jax.numpy as jnp
import numpy as np
from jax import lax
from jax.sharding import Mesh
from jax.sharding import PartitionSpec as P

EPS = 1e-06
INV_TAU = 10.0

ALL = ("xl", "c", "y", "z", "xh")
INNER = ("y", "z", "xh")
OUTER = ("xl", "c")
ROWS = ("c", "y", "z")
COLS = ("xl", "xh")


def block_exp(row_block, column_block):
    return jnp.exp(
        jnp.einsum("rd,cd->rc", row_block, column_block, preferred_element_type=jnp.float32)
        * INV_TAU
    )


def mixed_weights(exponent, row_total, column_total, row_first, column_first, rows_dev):
    row_offset = jnp.arange(exponent.shape[0], dtype=jnp.int32)[:, None] - row_first
    column_offset = jnp.arange(exponent.shape[1], dtype=jnp.int32)[None, :] - column_first
    diagonal = ((row_offset == column_offset) & (row_offset >= 0) & (row_offset < rows_dev)).astype(
        jnp.float32
    )
    return (
        0.5 * (exponent / row_total[:, None] + exponent / column_total[None, :]) - diagonal
    ).astype(jnp.bfloat16)


def column_terms(weights, row_block):
    return lax.dot_general(
        weights, row_block, (((0,), (0,)), ((), ())), preferred_element_type=jnp.float32
    )


def tree_sum(value, axes):
    for axis in axes:
        size = lax.axis_size(axis)
        step = 1
        while step < size:
            pairs = [(i, i ^ step) for i in range(size)]
            value = value + lax.ppermute(value, axis, pairs)
            step *= 2
    return value


def fetch_rows(queue, owner, slot):
    outer_count = lax.axis_size(OUTER)
    inner_count = lax.axis_size(INNER)
    rows_dev = slot.shape[0]
    feature_width = queue.shape[1]
    cap_member = max(2, 2 * rows_dev // inner_count)
    cap_group = inner_count * cap_member // outer_count
    owners_of = owner[:, 0]
    owner_member = owners_of % inner_count
    owner_group = owners_of // inner_count
    position = jnp.arange(rows_dev, dtype=jnp.int32)
    earlier = (owner_member[:, None] == owner_member[None, :]) & (
        position[None, :] < position[:, None]
    )
    member_place = owner_member * cap_member + jnp.sum(earlier.astype(jnp.int32), 1)
    request = jnp.stack(
        [
            jnp.full((inner_count * cap_member,), -1, jnp.int32).at[member_place].set(slot),
            jnp.full((inner_count * cap_member,), outer_count, jnp.int32)
            .at[member_place]
            .set(owner_group),
        ],
        1,
    ).reshape(inner_count, cap_member, 2)
    relay = lax.all_to_all(request, INNER, split_axis=0, concat_axis=0, tiled=True)
    relay_slot = relay[:, :, 0].reshape(-1)
    relay_group = relay[:, :, 1].reshape(-1)
    entry_index = jnp.arange(relay_slot.shape[0], dtype=jnp.int32)
    ahead = (relay_group[:, None] == relay_group[None, :]) & (
        entry_index[None, :] < entry_index[:, None]
    )
    group_place = relay_group * cap_group + jnp.sum(ahead.astype(jnp.int32), 1)
    asking = (
        jnp.full((outer_count * cap_group,), -1, jnp.int32)
        .at[group_place]
        .set(relay_slot, mode="drop")
    )
    asking = asking.reshape(outer_count, cap_group)
    asked = lax.all_to_all(asking, OUTER, split_axis=0, concat_axis=0, tiled=True)
    looked = jnp.take(queue, jnp.maximum(asked, 0), axis=0)
    looked = jnp.where((asked >= 0)[..., None], looked, jnp.zeros((), jnp.bfloat16))
    answered = lax.all_to_all(looked, OUTER, split_axis=0, concat_axis=0, tiled=True)
    answered = answered.reshape(outer_count * cap_group, feature_width)
    relayed = jnp.take(answered, jnp.minimum(group_place, outer_count * cap_group - 1), axis=0)
    relayed = jnp.where((relay_slot >= 0)[:, None], relayed, jnp.zeros((), jnp.bfloat16))
    relayed = relayed.reshape(inner_count, cap_member, feature_width)
    returned = lax.all_to_all(relayed, INNER, split_axis=0, concat_axis=0, tiled=True)
    return jnp.take(
        returned.reshape(inner_count * cap_member, feature_width), member_place, axis=0
    ).astype(jnp.float32)


def ring_pairs(size, step):
    return [(i, (i + step) % size) for i in range(size)]


def gather_columns(value, axes):
    size = lax.axis_size(axes)
    me = lax.axis_index(axes)
    parts = [value] + [lax.ppermute(value, axes, ring_pairs(size, k)) for k in range(1, size)]
    source = (me - jnp.arange(size, dtype=jnp.int32)) % size
    return jnp.take(jnp.stack(parts), source, axis=0).reshape((-1,) + value.shape[1:])


def scatter_columns(weights, row_block, axes, rows_dev):
    size = lax.axis_size(axes)
    me = lax.axis_index(axes)
    terms = column_terms(weights, row_block)
    total = lax.dynamic_slice_in_dim(terms, me * rows_dev, rows_dev, axis=0)
    for k in range(1, size):
        target = (me + k) % size
        piece = lax.dynamic_slice_in_dim(terms, target * rows_dev, rows_dev, axis=0)
        total = total + lax.ppermute(piece, axes, ring_pairs(size, k))
    return total


def shards(queue, pred, owner, slot):
    rows_dev = pred.shape[0]
    fetched = fetch_rows(queue, owner, slot)
    neighbour = (fetched * lax.rsqrt(jnp.sum(fetched * fetched, 1, keepdims=True) + EPS)).astype(
        jnp.bfloat16
    )
    predicted = pred.astype(jnp.float32)
    inverse = lax.rsqrt(jnp.sum(predicted * predicted, 1, keepdims=True) + EPS)
    queries = (predicted * inverse).astype(jnp.bfloat16)
    row_at = lax.axis_index(ROWS)
    column_at = lax.axis_index(COLS)
    row_block = lax.all_gather(neighbour, ROWS, axis=0, tiled=True)
    exponent = block_exp(row_block, gather_columns(queries, COLS))
    row_total = tree_sum(jnp.sum(exponent, 1), ROWS)
    column_total = tree_sum(jnp.sum(exponent, 0), COLS)
    weights = mixed_weights(
        exponent, row_total, column_total, row_at * rows_dev, column_at * rows_dev, rows_dev
    )
    dquery = scatter_columns(weights, row_block, COLS, rows_dev)
    dquery = dquery * INV_TAU
    radial = jnp.sum(predicted * dquery, 1, keepdims=True)
    return inverse * dquery - predicted * inverse * inverse * inverse * radial


def solution(mesh):
    axes = dict(zip(mesh.axis_names, mesh.devices.shape))
    outer, inner = axes["outer"], axes["inner"]
    fine = Mesh(
        np.asarray(mesh.devices).reshape(2, outer // 2, inner // 16, 8, 2), ALL
    )
    spec = P(ALL, None)
    in_specs = (spec, spec, spec, P(ALL))
    return jax.shard_map(shards, mesh=fine, in_specs=in_specs, out_specs=spec, check_vma=False)
```

```python
import jax
import jax.numpy as jnp
import numpy as np
from jax import lax
from jax.sharding import Mesh
from jax.sharding import PartitionSpec as P

EPS = 1e-06
INV_TAU = 10.0

ALL = ("xl", "c", "y", "z", "xh")
INNER = ("y", "z", "xh")
OUTER = ("xl", "c")
ROWS = ("c", "y", "z")
COLS = ("xl", "xh")


def block_exp(row_block, column_block):
    return jnp.exp(
        jnp.einsum("rd,cd->rc", row_block, column_block, preferred_element_type=jnp.float32)
        * INV_TAU
    )


def mixed_weights(exponent, row_total, column_total, row_first, column_first, rows_dev):
    row_offset = jnp.arange(exponent.shape[0], dtype=jnp.int32)[:, None] - row_first
    column_offset = jnp.arange(exponent.shape[1], dtype=jnp.int32)[None, :] - column_first
    diagonal = ((row_offset == column_offset) & (row_offset >= 0) & (row_offset < rows_dev)).astype(
        jnp.float32
    )
    row_scale = 0.5 / row_total
    column_scale = 0.5 / column_total
    return (exponent * (row_scale[:, None] + column_scale[None, :]) - diagonal).astype(jnp.bfloat16)


def column_terms(weights, row_block):
    return lax.dot_general(
        weights, row_block, (((0,), (0,)), ((), ())), preferred_element_type=jnp.float32
    )


def tree_sum(value, axes):
    for axis in axes:
        size = lax.axis_size(axis)
        step = 1
        while step < size:
            pairs = [(i, i ^ step) for i in range(size)]
            value = value + lax.ppermute(value, axis, pairs)
            step *= 2
    return value


def fetch_rows(queue, owner, slot):
    outer_count = lax.axis_size(OUTER)
    inner_count = lax.axis_size(INNER)
    rows_dev = slot.shape[0]
    feature_width = queue.shape[1]
    cap_member = max(2, 2 * rows_dev // inner_count)
    cap_group = inner_count * cap_member // outer_count
    owners_of = owner[:, 0]
    owner_member = owners_of % inner_count
    owner_group = owners_of // inner_count
    position = jnp.arange(rows_dev, dtype=jnp.int32)
    earlier = (owner_member[:, None] == owner_member[None, :]) & (
        position[None, :] < position[:, None]
    )
    member_place = owner_member * cap_member + jnp.sum(earlier.astype(jnp.int32), 1)
    request = jnp.stack(
        [
            jnp.full((inner_count * cap_member,), -1, jnp.int32).at[member_place].set(slot),
            jnp.full((inner_count * cap_member,), outer_count, jnp.int32)
            .at[member_place]
            .set(owner_group),
        ],
        1,
    ).reshape(inner_count, cap_member, 2)
    relay = lax.all_to_all(request, INNER, split_axis=0, concat_axis=0, tiled=True)
    relay_slot = relay[:, :, 0].reshape(-1)
    relay_group = relay[:, :, 1].reshape(-1)
    entry_index = jnp.arange(relay_slot.shape[0], dtype=jnp.int32)
    ahead = (relay_group[:, None] == relay_group[None, :]) & (
        entry_index[None, :] < entry_index[:, None]
    )
    group_place = relay_group * cap_group + jnp.sum(ahead.astype(jnp.int32), 1)
    asking = (
        jnp.full((outer_count * cap_group,), -1, jnp.int32)
        .at[group_place]
        .set(relay_slot, mode="drop")
    )
    asking = asking.reshape(outer_count, cap_group)
    asked = lax.all_to_all(asking, OUTER, split_axis=0, concat_axis=0, tiled=True)
    looked = jnp.take(queue, jnp.maximum(asked, 0), axis=0)
    looked = jnp.where((asked >= 0)[..., None], looked, jnp.zeros((), jnp.bfloat16))
    answered = lax.all_to_all(looked, OUTER, split_axis=0, concat_axis=0, tiled=True)
    answered = answered.reshape(outer_count * cap_group, feature_width)
    relayed = jnp.take(answered, jnp.minimum(group_place, outer_count * cap_group - 1), axis=0)
    relayed = jnp.where((relay_slot >= 0)[:, None], relayed, jnp.zeros((), jnp.bfloat16))
    relayed = relayed.reshape(inner_count, cap_member, feature_width)
    returned = lax.all_to_all(relayed, INNER, split_axis=0, concat_axis=0, tiled=True)
    return jnp.take(
        returned.reshape(inner_count * cap_member, feature_width), member_place, axis=0
    ).astype(jnp.float32)


def ring_pairs(size, step):
    return [(i, (i + step) % size) for i in range(size)]


def gather_columns(value, axes):
    size = lax.axis_size(axes)
    me = lax.axis_index(axes)
    parts = [value] + [lax.ppermute(value, axes, ring_pairs(size, k)) for k in range(1, size)]
    source = (me - jnp.arange(size, dtype=jnp.int32)) % size
    return jnp.take(jnp.stack(parts), source, axis=0).reshape((-1,) + value.shape[1:])


def scatter_columns(weights, row_block, axes, rows_dev):
    size = lax.axis_size(axes)
    me = lax.axis_index(axes)
    terms = column_terms(weights, row_block)
    total = lax.dynamic_slice_in_dim(terms, me * rows_dev, rows_dev, axis=0)
    for k in range(1, size):
        target = (me + k) % size
        piece = lax.dynamic_slice_in_dim(terms, target * rows_dev, rows_dev, axis=0)
        total = total + lax.ppermute(piece, axes, ring_pairs(size, k))
    return total


def shards(queue, pred, owner, slot):
    rows_dev = pred.shape[0]
    fetched = fetch_rows(queue, owner, slot)
    neighbour = (fetched * lax.rsqrt(jnp.sum(fetched * fetched, 1, keepdims=True) + EPS)).astype(
        jnp.bfloat16
    )
    predicted = pred.astype(jnp.float32)
    inverse = lax.rsqrt(jnp.sum(predicted * predicted, 1, keepdims=True) + EPS)
    queries = (predicted * inverse).astype(jnp.bfloat16)
    row_at = lax.axis_index(ROWS)
    column_at = lax.axis_index(COLS)
    row_block = lax.all_gather(neighbour, ROWS, axis=0, tiled=True)
    exponent = block_exp(row_block, gather_columns(queries, COLS))
    row_total = tree_sum(jnp.sum(exponent, 1), ROWS)
    column_total = tree_sum(jnp.sum(exponent, 0), COLS)
    weights = mixed_weights(
        exponent, row_total, column_total, row_at * rows_dev, column_at * rows_dev, rows_dev
    )
    dquery = scatter_columns(weights, row_block, COLS, rows_dev)
    dquery = dquery * INV_TAU
    radial = jnp.sum(predicted * dquery, 1, keepdims=True)
    return inverse * dquery - predicted * inverse * inverse * inverse * radial


def solution(mesh):
    axes = dict(zip(mesh.axis_names, mesh.devices.shape))
    outer, inner = axes["outer"], axes["inner"]
    fine = Mesh(
        np.asarray(mesh.devices).reshape(2, outer // 2, inner // 16, 8, 2), ALL
    )
    spec = P(ALL, None)
    in_specs = (spec, spec, spec, P(ALL))
    return jax.shard_map(shards, mesh=fine, in_specs=in_specs, out_specs=spec, check_vma=False)
```

```python
import jax
import jax.numpy as jnp
import numpy as np
from jax import lax
from jax.sharding import Mesh
from jax.sharding import PartitionSpec as P

EPS = 1e-06
INV_TAU = 10.0

ALL = ("xl", "c", "y", "z", "xh")
INNER = ("y", "z", "xh")
OUTER = ("xl", "c")
ROWS = ("c", "y", "z")
COLS = ("xl", "xh")


def block_exp(row_block, column_block):
    return jnp.exp(
        jnp.einsum("rd,cd->rc", row_block, column_block, preferred_element_type=jnp.float32)
        * INV_TAU
    )


def mixed_weights(exponent, row_total, column_total, row_first, column_first, rows_dev):
    row_offset = jnp.arange(exponent.shape[0], dtype=jnp.int32)[:, None] - row_first
    column_offset = jnp.arange(exponent.shape[1], dtype=jnp.int32)[None, :] - column_first
    diagonal = ((row_offset == column_offset) & (row_offset >= 0) & (row_offset < rows_dev)).astype(
        jnp.float32
    )
    row_scale = 0.5 / row_total
    column_scale = 0.5 / column_total
    return (exponent * (row_scale[:, None] + column_scale[None, :]) - diagonal).astype(jnp.bfloat16)


def column_terms(weights, row_block):
    return lax.dot_general(
        weights, row_block, (((0,), (0,)), ((), ())), preferred_element_type=jnp.float32
    )


def tree_sum(value, axes):
    for axis in axes:
        size = lax.axis_size(axis)
        if size == 4:
            me = lax.axis_index(axis)
            parts = [value] + [lax.ppermute(value, axis, ring_pairs(size, k)) for k in range(1, size)]
            ordered = jnp.take(jnp.stack(parts), (me - jnp.arange(size, dtype=jnp.int32)) % size, axis=0)
            value = ordered[0]
            for k in range(1, size):
                value = value + ordered[k]
            continue
        step = 1
        while step < size:
            pairs = [(i, i ^ step) for i in range(size)]
            value = value + lax.ppermute(value, axis, pairs)
            step *= 2
    return value


def fetch_rows(queue, owner, slot):
    outer_count = lax.axis_size(OUTER)
    inner_count = lax.axis_size(INNER)
    rows_dev = slot.shape[0]
    feature_width = queue.shape[1]
    cap_member = max(2, 2 * rows_dev // inner_count)
    cap_group = inner_count * cap_member // outer_count
    owners_of = owner[:, 0]
    owner_member = owners_of % inner_count
    owner_group = owners_of // inner_count
    position = jnp.arange(rows_dev, dtype=jnp.int32)
    earlier = (owner_member[:, None] == owner_member[None, :]) & (
        position[None, :] < position[:, None]
    )
    member_place = owner_member * cap_member + jnp.sum(earlier.astype(jnp.int32), 1)
    request = jnp.stack(
        [
            jnp.full((inner_count * cap_member,), -1, jnp.int32).at[member_place].set(slot),
            jnp.full((inner_count * cap_member,), outer_count, jnp.int32)
            .at[member_place]
            .set(owner_group),
        ],
        1,
    ).reshape(inner_count, cap_member, 2)
    relay = lax.all_to_all(request, INNER, split_axis=0, concat_axis=0, tiled=True)
    relay_slot = relay[:, :, 0].reshape(-1)
    relay_group = relay[:, :, 1].reshape(-1)
    entry_index = jnp.arange(relay_slot.shape[0], dtype=jnp.int32)
    ahead = (relay_group[:, None] == relay_group[None, :]) & (
        entry_index[None, :] < entry_index[:, None]
    )
    group_place = relay_group * cap_group + jnp.sum(ahead.astype(jnp.int32), 1)
    asking = (
        jnp.full((outer_count * cap_group,), -1, jnp.int32)
        .at[group_place]
        .set(relay_slot, mode="drop")
    )
    asking = asking.reshape(outer_count, cap_group)
    asked = lax.all_to_all(asking, OUTER, split_axis=0, concat_axis=0, tiled=True)
    looked = jnp.take(queue, jnp.maximum(asked, 0), axis=0)
    looked = jnp.where((asked >= 0)[..., None], looked, jnp.zeros((), jnp.bfloat16))
    answered = lax.all_to_all(looked, OUTER, split_axis=0, concat_axis=0, tiled=True)
    answered = answered.reshape(outer_count * cap_group, feature_width)
    relayed = jnp.take(answered, jnp.minimum(group_place, outer_count * cap_group - 1), axis=0)
    relayed = jnp.where((relay_slot >= 0)[:, None], relayed, jnp.zeros((), jnp.bfloat16))
    relayed = relayed.reshape(inner_count, cap_member, feature_width)
    returned = lax.all_to_all(relayed, INNER, split_axis=0, concat_axis=0, tiled=True)
    return jnp.take(
        returned.reshape(inner_count * cap_member, feature_width), member_place, axis=0
    ).astype(jnp.float32)


def ring_pairs(size, step):
    return [(i, (i + step) % size) for i in range(size)]


def gather_columns(value, axes):
    size = lax.axis_size(axes)
    me = lax.axis_index(axes)
    parts = [value] + [lax.ppermute(value, axes, ring_pairs(size, k)) for k in range(1, size)]
    source = (me - jnp.arange(size, dtype=jnp.int32)) % size
    return jnp.take(jnp.stack(parts), source, axis=0).reshape((-1,) + value.shape[1:])


def scatter_columns(weights, row_block, axes, rows_dev):
    size = lax.axis_size(axes)
    me = lax.axis_index(axes)
    terms = column_terms(weights, row_block)
    total = lax.dynamic_slice_in_dim(terms, me * rows_dev, rows_dev, axis=0)
    for k in range(1, size):
        target = (me + k) % size
        piece = lax.dynamic_slice_in_dim(terms, target * rows_dev, rows_dev, axis=0)
        total = total + lax.ppermute(piece, axes, ring_pairs(size, k))
    return total


def shards(queue, pred, owner, slot):
    rows_dev = pred.shape[0]
    fetched = fetch_rows(queue, owner, slot)
    neighbour = (fetched * lax.rsqrt(jnp.sum(fetched * fetched, 1, keepdims=True) + EPS)).astype(
        jnp.bfloat16
    )
    predicted = pred.astype(jnp.float32)
    inverse = lax.rsqrt(jnp.sum(predicted * predicted, 1, keepdims=True) + EPS)
    queries = (predicted * inverse).astype(jnp.bfloat16)
    row_at = lax.axis_index(ROWS)
    column_at = lax.axis_index(COLS)
    row_block = lax.all_gather(neighbour, ROWS, axis=0, tiled=True)
    exponent = block_exp(row_block, gather_columns(queries, COLS))
    row_total = tree_sum(jnp.sum(exponent, 1), ROWS)
    column_total = tree_sum(jnp.sum(exponent, 0), COLS)
    weights = mixed_weights(
        exponent, row_total, column_total, row_at * rows_dev, column_at * rows_dev, rows_dev
    )
    dquery = scatter_columns(weights, row_block, COLS, rows_dev)
    dquery = dquery * INV_TAU
    radial = jnp.sum(predicted * dquery, 1, keepdims=True)
    return inverse * dquery - predicted * inverse * inverse * inverse * radial


def solution(mesh):
    axes = dict(zip(mesh.axis_names, mesh.devices.shape))
    outer, inner = axes["outer"], axes["inner"]
    fine = Mesh(
        np.asarray(mesh.devices).reshape(2, outer // 2, inner // 16, 8, 2), ALL
    )
    spec = P(ALL, None)
    in_specs = (spec, spec, spec, P(ALL))
    return jax.shard_map(shards, mesh=fine, in_specs=in_specs, out_specs=spec, check_vma=False)
```

```python
import jax
import jax.numpy as jnp
import numpy as np
from jax import lax
from jax.sharding import Mesh
from jax.sharding import PartitionSpec as P

EPS = 1e-06
INV_TAU = 10.0

ALL = ("xl", "c", "y", "z", "xh")
INNER = ("y", "z", "xh")
OUTER = ("xl", "c")
ROWS = ("c", "y", "z")
COLS = ("xl", "xh")


def block_exp(row_block, column_block):
    return jnp.exp(
        jnp.einsum("rd,cd->rc", row_block, column_block, preferred_element_type=jnp.float32)
        * INV_TAU
    )


def mixed_weights(exponent, row_total, column_total, row_first, column_first, rows_dev):
    row_offset = jnp.arange(exponent.shape[0], dtype=jnp.int32)[:, None] - row_first
    column_offset = jnp.arange(exponent.shape[1], dtype=jnp.int32)[None, :] - column_first
    diagonal = ((row_offset == column_offset) & (row_offset >= 0) & (row_offset < rows_dev)).astype(
        jnp.float32
    )
    row_scale = 0.5 / row_total
    column_scale = 0.5 / column_total
    return (exponent * (row_scale[:, None] + column_scale[None, :]) - diagonal).astype(jnp.bfloat16)


def column_terms(weights, row_block):
    return lax.dot_general(
        weights, row_block, (((0,), (0,)), ((), ())), preferred_element_type=jnp.float32
    )


def tree_sum(value, axes):
    for axis in axes:
        size = lax.axis_size(axis)
        if size == 4:
            me = lax.axis_index(axis)
            parts = [value] + [lax.ppermute(value, axis, ring_pairs(size, k)) for k in range(1, size)]
            ordered = jnp.take(jnp.stack(parts), (me - jnp.arange(size, dtype=jnp.int32)) % size, axis=0)
            value = ordered[0]
            for k in range(1, size):
                value = value + ordered[k]
            continue
        step = 1
        while step < size:
            pairs = [(i, i ^ step) for i in range(size)]
            value = value + lax.ppermute(value, axis, pairs)
            step *= 2
    return value


def fetch_rows(queue, owner, slot):
    outer_count = lax.axis_size(OUTER)
    inner_count = lax.axis_size(INNER)
    rows_dev = slot.shape[0]
    feature_width = queue.shape[1]
    cap_member = max(2, 2 * rows_dev // inner_count)
    cap_group = inner_count * cap_member // outer_count
    owners_of = owner[:, 0]
    owner_member = owners_of % inner_count
    owner_group = owners_of // inner_count
    position = jnp.arange(rows_dev, dtype=jnp.int32)
    earlier = (owner_member[:, None] == owner_member[None, :]) & (
        position[None, :] < position[:, None]
    )
    member_place = owner_member * cap_member + jnp.sum(earlier.astype(jnp.int32), 1)
    request = jnp.stack(
        [
            jnp.full((inner_count * cap_member,), -1, jnp.int32).at[member_place].set(slot),
            jnp.full((inner_count * cap_member,), outer_count, jnp.int32)
            .at[member_place]
            .set(owner_group),
        ],
        1,
    ).reshape(inner_count, cap_member, 2)
    relay = lax.all_to_all(request, INNER, split_axis=0, concat_axis=0, tiled=True)
    relay_slot = relay[:, :, 0].reshape(-1)
    relay_group = relay[:, :, 1].reshape(-1)
    entry_index = jnp.arange(relay_slot.shape[0], dtype=jnp.int32)
    ahead = (relay_group[:, None] == relay_group[None, :]) & (
        entry_index[None, :] < entry_index[:, None]
    )
    group_place = relay_group * cap_group + jnp.sum(ahead.astype(jnp.int32), 1)
    asking = (
        jnp.full((outer_count * cap_group,), -1, jnp.int32)
        .at[group_place]
        .set(relay_slot, mode="drop")
    )
    asking = asking.reshape(outer_count, cap_group)
    asked = lax.all_to_all(asking, OUTER, split_axis=0, concat_axis=0, tiled=True)
    looked = jnp.take(queue, jnp.maximum(asked, 0), axis=0)
    looked = jnp.where((asked >= 0)[..., None], looked, jnp.zeros((), jnp.bfloat16))
    answered = lax.all_to_all(looked, OUTER, split_axis=0, concat_axis=0, tiled=True)
    answered = answered.reshape(outer_count * cap_group, feature_width)
    relayed = jnp.take(answered, jnp.minimum(group_place, outer_count * cap_group - 1), axis=0)
    relayed = jnp.where((relay_slot >= 0)[:, None], relayed, jnp.zeros((), jnp.bfloat16))
    relayed = relayed.reshape(inner_count, cap_member, feature_width)
    returned = lax.all_to_all(relayed, INNER, split_axis=0, concat_axis=0, tiled=True)
    return jnp.take(
        returned.reshape(inner_count * cap_member, feature_width), member_place, axis=0
    ).astype(jnp.float32)


def ring_pairs(size, step):
    return [(i, (i + step) % size) for i in range(size)]


def gather_columns(value, axes):
    size = lax.axis_size(axes)
    me = lax.axis_index(axes)
    parts = [value] + [lax.ppermute(value, axes, ring_pairs(size, k)) for k in range(1, size)]
    source = (me - jnp.arange(size, dtype=jnp.int32)) % size
    return jnp.take(jnp.stack(parts), source, axis=0).reshape((-1,) + value.shape[1:])


def scatter_columns(weights, row_block, axes, rows_dev):
    size = lax.axis_size(axes)
    me = lax.axis_index(axes)
    terms = column_terms(weights, row_block)
    total = lax.dynamic_slice_in_dim(terms, me * rows_dev, rows_dev, axis=0)
    for k in range(1, size):
        target = (me + k) % size
        piece = lax.dynamic_slice_in_dim(terms, target * rows_dev, rows_dev, axis=0)
        sent = lax.ppermute(piece.astype(jnp.bfloat16), axes, ring_pairs(size, k))
        total = total + sent.astype(jnp.float32)
    return total


def shards(queue, pred, owner, slot):
    rows_dev = pred.shape[0]
    fetched = fetch_rows(queue, owner, slot)
    neighbour = (fetched * lax.rsqrt(jnp.sum(fetched * fetched, 1, keepdims=True) + EPS)).astype(
        jnp.bfloat16
    )
    predicted = pred.astype(jnp.float32)
    inverse = lax.rsqrt(jnp.sum(predicted * predicted, 1, keepdims=True) + EPS)
    queries = (predicted * inverse).astype(jnp.bfloat16)
    row_at = lax.axis_index(ROWS)
    column_at = lax.axis_index(COLS)
    row_block = lax.all_gather(neighbour, ROWS, axis=0, tiled=True)
    exponent = block_exp(row_block, gather_columns(queries, COLS))
    row_total = tree_sum(jnp.sum(exponent, 1), ROWS)
    column_total = tree_sum(jnp.sum(exponent, 0), COLS)
    weights = mixed_weights(
        exponent, row_total, column_total, row_at * rows_dev, column_at * rows_dev, rows_dev
    )
    dquery = scatter_columns(weights, row_block, COLS, rows_dev)
    dquery = dquery * INV_TAU
    radial = jnp.sum(predicted * dquery, 1, keepdims=True)
    return inverse * dquery - predicted * inverse * inverse * inverse * radial


def solution(mesh):
    axes = dict(zip(mesh.axis_names, mesh.devices.shape))
    outer, inner = axes["outer"], axes["inner"]
    fine = Mesh(
        np.asarray(mesh.devices).reshape(2, outer // 2, inner // 16, 8, 2), ALL
    )
    spec = P(ALL, None)
    in_specs = (spec, spec, spec, P(ALL))
    return jax.shard_map(shards, mesh=fine, in_specs=in_specs, out_specs=spec, check_vma=False)
```

```python
import jax
import jax.numpy as jnp
import numpy as np
from jax import lax
from jax.sharding import Mesh
from jax.sharding import PartitionSpec as P

EPS = 1e-06
INV_TAU = 10.0

ALL = ("xl", "c", "y", "z", "xh")
INNER = ("y", "z", "xh")
OUTER = ("xl", "c")
ROWS = ("c", "y", "z")
COLS = ("xl", "xh")


def block_exp(row_block, column_block):
    return jnp.exp(
        jnp.einsum("rd,cd->rc", row_block, column_block, preferred_element_type=jnp.float32)
        * INV_TAU
    )


def mixed_weights(exponent, row_total, column_total, row_first, column_first, rows_dev):
    row_offset = jnp.arange(exponent.shape[0], dtype=jnp.int32)[:, None] - row_first
    column_offset = jnp.arange(exponent.shape[1], dtype=jnp.int32)[None, :] - column_first
    diagonal = ((row_offset == column_offset) & (row_offset >= 0) & (row_offset < rows_dev)).astype(
        jnp.float32
    )
    row_scale = 0.5 / row_total
    column_scale = 0.5 / column_total
    return (exponent * (row_scale[:, None] + column_scale[None, :]) - diagonal).astype(jnp.bfloat16)


def column_terms(weights, row_block):
    return lax.dot_general(
        weights, row_block, (((0,), (0,)), ((), ())), preferred_element_type=jnp.float32
    )


def tree_sum(value, axes):
    for axis in axes:
        size = lax.axis_size(axis)
        if size == 4:
            me = lax.axis_index(axis)
            parts = [value] + [lax.ppermute(value, axis, ring_pairs(size, k)) for k in range(1, size)]
            ordered = jnp.take(jnp.stack(parts), (me - jnp.arange(size, dtype=jnp.int32)) % size, axis=0)
            value = ordered[0]
            for k in range(1, size):
                value = value + ordered[k]
            continue
        step = 1
        while step < size:
            pairs = [(i, i ^ step) for i in range(size)]
            value = value + lax.ppermute(value, axis, pairs)
            step *= 2
    return value


def fetch_rows(queue, owner, slot):
    outer_count = lax.axis_size(OUTER)
    inner_count = lax.axis_size(INNER)
    rows_dev = slot.shape[0]
    feature_width = queue.shape[1]
    cap_member = max(2, 2 * rows_dev // inner_count)
    cap_group = inner_count * cap_member // outer_count
    owners_of = owner[:, 0]
    owner_member = owners_of % inner_count
    owner_group = owners_of // inner_count
    position = jnp.arange(rows_dev, dtype=jnp.int32)
    earlier = (owner_member[:, None] == owner_member[None, :]) & (
        position[None, :] < position[:, None]
    )
    member_place = owner_member * cap_member + jnp.sum(earlier.astype(jnp.int32), 1)
    request = jnp.stack(
        [
            jnp.full((inner_count * cap_member,), -1, jnp.int32).at[member_place].set(slot),
            jnp.full((inner_count * cap_member,), outer_count, jnp.int32)
            .at[member_place]
            .set(owner_group),
        ],
        1,
    ).reshape(inner_count, cap_member, 2)
    relay = lax.all_to_all(request, INNER, split_axis=0, concat_axis=0, tiled=True)
    relay_slot = relay[:, :, 0].reshape(-1)
    relay_group = relay[:, :, 1].reshape(-1)
    entry_index = jnp.arange(relay_slot.shape[0], dtype=jnp.int32)
    ahead = (relay_group[:, None] == relay_group[None, :]) & (
        entry_index[None, :] < entry_index[:, None]
    )
    group_place = relay_group * cap_group + jnp.sum(ahead.astype(jnp.int32), 1)
    asking = (
        jnp.full((outer_count * cap_group,), -1, jnp.int32)
        .at[group_place]
        .set(relay_slot, mode="drop")
    )
    asking = asking.reshape(outer_count, cap_group)
    asked = lax.all_to_all(asking, OUTER, split_axis=0, concat_axis=0, tiled=True)
    looked = jnp.take(queue, jnp.maximum(asked, 0), axis=0)
    answered = lax.all_to_all(looked, OUTER, split_axis=0, concat_axis=0, tiled=True)
    answered = answered.reshape(outer_count * cap_group, feature_width)
    relayed = jnp.take(answered, jnp.minimum(group_place, outer_count * cap_group - 1), axis=0)
    relayed = relayed.reshape(inner_count, cap_member, feature_width)
    returned = lax.all_to_all(relayed, INNER, split_axis=0, concat_axis=0, tiled=True)
    return jnp.take(
        returned.reshape(inner_count * cap_member, feature_width), member_place, axis=0
    ).astype(jnp.float32)


def ring_pairs(size, step):
    return [(i, (i + step) % size) for i in range(size)]


def gather_columns(value, axes):
    size = lax.axis_size(axes)
    me = lax.axis_index(axes)
    parts = [value] + [lax.ppermute(value, axes, ring_pairs(size, k)) for k in range(1, size)]
    source = (me - jnp.arange(size, dtype=jnp.int32)) % size
    return jnp.take(jnp.stack(parts), source, axis=0).reshape((-1,) + value.shape[1:])


def scatter_columns(weights, row_block, axes, rows_dev):
    size = lax.axis_size(axes)
    me = lax.axis_index(axes)
    terms = column_terms(weights, row_block)
    total = lax.dynamic_slice_in_dim(terms, me * rows_dev, rows_dev, axis=0)
    for k in range(1, size):
        target = (me + k) % size
        piece = lax.dynamic_slice_in_dim(terms, target * rows_dev, rows_dev, axis=0)
        total = total + lax.ppermute(piece, axes, ring_pairs(size, k))
    return total


def shards(queue, pred, owner, slot):
    rows_dev = pred.shape[0]
    fetched = fetch_rows(queue, owner, slot)
    neighbour = (fetched * lax.rsqrt(jnp.sum(fetched * fetched, 1, keepdims=True) + EPS)).astype(
        jnp.bfloat16
    )
    predicted = pred.astype(jnp.float32)
    inverse = lax.rsqrt(jnp.sum(predicted * predicted, 1, keepdims=True) + EPS)
    queries = (predicted * inverse).astype(jnp.bfloat16)
    row_at = lax.axis_index(ROWS)
    column_at = lax.axis_index(COLS)
    row_block = lax.all_gather(neighbour, ROWS, axis=0, tiled=True)
    exponent = block_exp(row_block, gather_columns(queries, COLS))
    row_total = tree_sum(jnp.sum(exponent, 1), ROWS)
    column_total = tree_sum(jnp.sum(exponent, 0), COLS)
    weights = mixed_weights(
        exponent, row_total, column_total, row_at * rows_dev, column_at * rows_dev, rows_dev
    )
    dquery = scatter_columns(weights, row_block, COLS, rows_dev)
    dquery = dquery * INV_TAU
    radial = jnp.sum(predicted * dquery, 1, keepdims=True)
    return inverse * dquery - predicted * inverse * inverse * inverse * radial


def solution(mesh):
    axes = dict(zip(mesh.axis_names, mesh.devices.shape))
    outer, inner = axes["outer"], axes["inner"]
    fine = Mesh(
        np.asarray(mesh.devices).reshape(2, outer // 2, inner // 16, 8, 2), ALL
    )
    spec = P(ALL, None)
    in_specs = (spec, spec, spec, P(ALL))
    return jax.shard_map(shards, mesh=fine, in_specs=in_specs, out_specs=spec, check_vma=False)
```
